256 devices in a mesh: row: 16 (over z_hi, y, core), col: 16 (over x, z_lo).
Axes of the slice: x: 4, y: 4, z: 8 (z_hi: 2, z_lo: 4; z = z_hi * 4 + z_lo), core: 2. Of those that a mesh axis runs over, the one named last changes fastest.
Arguments:
- coefficients: float32 [8192, 8192], P('row', 'col'), may hold values from -6 to 6
- alpha_pattern: int32 [16, 10], P('row'), may hold values from 0 to 15, all different within a row
- alpha_count: int32 [16], P('row'), may hold values from 1 to 10
- alpha_blocks: bfloat16 [16, 10, 512, 512], P('row'), may hold values from -0.078125 to 0.078125
- beta_pattern: int32 [16, 10], P('col'), may hold values from 0 to 15, all different within a row
- beta_count: int32 [16], P('col'), may hold values from 1 to 10
- beta_blocks: bfloat16 [16, 10, 512, 512], P('col'), may hold values from -0.078125 to 0.078125
Outputs:
- sigma: float32 [8192, 8192], P('row', 'col')
The draws below stay inside these ranges and needn't reach their ends.
Inputs may be any that keep to these rules, and one draw needn't show every extreme that they name: `alpha_pattern`: each row lists 10 different blocks, and every block stands in some row. `beta_pattern`: each row lists 10 different blocks, and every block stands in some row.
All inputs are finite; a program needn't handle non-finite values.
Results may differ from the reference program's by a relative error of at most 0.0029.
Values may be sent and summed in bfloat16 or wider, within the bound.
No kernel may reach another device: no remote copies, remote signals or barrier semaphores. Data moves between devices by JAX's collectives and lax.ppermute only.
A program may use at most 128 MiB of HBM per device.

```python
import jax
import jax.numpy as jnp
from jax import lax

NS = 8192
BLK = 512
K = 10
NBLK = 16


def plant(entries, key, low, high):
    shape = entries.shape
    index_at = [jax.random.randint(jax.random.fold_in(key, axis), (), 0, shape[axis]) for axis in range(len(shape))]
    entries = entries.at[tuple(index_at)].set(low)
    longest = shape.index(max(shape))
    index_at[longest] = (index_at[longest] + 1) % shape[longest]
    return entries.at[tuple(index_at)].set(high)


def shard_levels(key, shape, shards, low, high):
    def one(position, parts):
        draws = jax.random.uniform(jax.random.fold_in(jax.random.fold_in(key, 6), position), (parts,), jnp.float32, low / len(shards), high / len(shards))
        return jnp.repeat(jnp.exp(draws), shape[position] // parts).reshape((-1,) + (1,) * (len(shape) - position - 1))

    gain = one(*shards[0])
    for cut in shards[1:]:
        gain = gain * one(*cut)
    return gain


def choose_distinct(key, rows, amount, top, lift):
    sequence = jax.random.permutation(jax.random.fold_in(key, 1), amount)
    boost = sequence
    for power in range(3):
        boost = boost * boost // amount
    boost = boost * lift // amount
    lots = jax.random.randint(jax.random.fold_in(key, 2), (rows, amount), 0, 4096) + boost
    holders = jax.random.permutation(jax.random.fold_in(key, 3), rows)[jnp.arange(amount) % rows]
    lots = jnp.where(jnp.arange(rows)[:, None] == holders[None, :], 1 << 14, lots)
    priority = lots * amount + jnp.arange(amount)
    return lax.top_k(priority.astype(jnp.int32), top)[1].astype(jnp.int32)


def gaussian(stream_key, extent, deviation, limit, pieces=(), kind=jnp.bfloat16):
    result = jax.random.normal(stream_key, extent, jnp.float32) * deviation
    if len(pieces) > 0:
        result = shard_levels(stream_key, extent, pieces, -0.22, 0.18) * result
    return jnp.clip(result, min=-limit, max=limit).astype(kind)


def setup_inputs(seed: int = 0) -> dict:
    seeds = jax.random.split(jax.random.key(seed), 8)
    coefficients = gaussian(seeds[0], (NS, NS), 1.0, 6.0, ((0, 16), (1, 16)), jnp.float32)
    alpha_pattern = choose_distinct(seeds[1], NBLK, NBLK, K, 5120)
    alpha_count = plant(jax.random.randint(seeds[2], (NBLK,), 1, K + 1), jax.random.fold_in(seeds[2], 1), 1, K).astype(jnp.int32)
    alpha_blocks = gaussian(seeds[3], (NBLK, K, BLK, BLK), (BLK * K) ** -0.5, 0.078125, ((0, 16),))
    beta_pattern = choose_distinct(seeds[4], NBLK, NBLK, K, 5120)
    beta_count = plant(jax.random.randint(seeds[5], (NBLK,), 1, K + 1), jax.random.fold_in(seeds[5], 1), 1, K).astype(jnp.int32)
    beta_blocks = gaussian(seeds[6], (NBLK, K, BLK, BLK), (BLK * K) ** -0.5, 0.078125, ((0, 16),))
    return {"coefficients": coefficients, "alpha_pattern": alpha_pattern, "alpha_count": alpha_count, "alpha_blocks": alpha_blocks, "beta_pattern": beta_pattern, "beta_count": beta_count, "beta_blocks": beta_blocks}


def reference(coefficients, alpha_pattern, alpha_count, alpha_blocks, beta_pattern, beta_count, beta_blocks):
    coeff_bf = coefficients.astype(jnp.bfloat16)
    row_blocks = coeff_bf.reshape(NBLK, BLK, NS)
    col_blocks = coeff_bf.reshape(NS, NBLK, BLK)
    slot_ids = jnp.arange(K, dtype=jnp.int32)

    def alpha_row(index):
        mask = (slot_ids < alpha_count[index]).astype(jnp.float32)
        weights = alpha_blocks[index].astype(jnp.float32) * mask[:, None, None]
        picked = row_blocks[alpha_pattern[index]].astype(jnp.float32)
        return jnp.einsum("tab,tbn->an", weights, picked)

    def beta_row(index):
        mask = (slot_ids < beta_count[index]).astype(jnp.float32)
        weights = beta_blocks[index].astype(jnp.float32) * mask[:, None, None]
        picked = col_blocks[:, beta_pattern[index], :].astype(jnp.float32)
        return jnp.einsum("ntk,tck->nc", picked, weights)

    indices = jnp.arange(NBLK, dtype=jnp.int32)
    alpha_term = lax.map(alpha_row, indices).reshape(NS, NS)
    beta_term = jnp.transpose(lax.map(beta_row, indices), (1, 0, 2)).reshape(NS, NS)
    return alpha_term + beta_term
```

```python
import jax
import jax.numpy as jnp
from jax import lax
from jax.sharding import Mesh, PartitionSpec as P

ROW = ("zh", "y", "core")
COL = ("x", "zl")
ROWMODE = "pp"
COLMODE = "pp"


def slot_mask(count, slots):
    return lax.broadcasted_iota(jnp.int32, (count.shape[0], slots), 1) < count[:, None]


def shifts(x, axis):
    n = lax.axis_size(axis)
    out = [x]
    for s in range(1, n):
        out.append(lax.ppermute(x, axis, [(i, (i + s) % n) for i in range(n)]))
    return jnp.stack(out, axis=0)


def row_tiles(t):
    if ROWMODE == "sc":
        slab = lax.all_gather(t, ROW, axis=0, tiled=False)
        return slab.reshape((-1,) + t.shape), lambda p: p
    zh = lax.axis_index("zh"); y = lax.axis_index("y"); core = lax.axis_index("core")
    a1 = shifts(t, "zh")
    a2 = shifts(a1, "y")
    a3 = shifts(a2, "core")
    slab = a3.reshape((-1,) + t.shape)
    def pos(p):
        k1 = (p // 8) ^ zh
        k2 = (y - (p // 2) % 4) % 4
        k3 = (p % 2) ^ core
        return k3 * 8 + k2 * 2 + k1
    return slab, pos


def col_tiles(t):
    if COLMODE == "sc":
        slab = lax.all_gather(t, COL, axis=0, tiled=False)
        return slab.reshape((-1,) + t.shape), lambda q: q
    x = lax.axis_index("x"); zl = lax.axis_index("zl")
    b1 = shifts(t, "zl")
    b2 = shifts(b1, "x")
    slab = b2.reshape((-1,) + t.shape)
    def pos(q):
        k1 = (zl - q % 4) % 4
        k2 = (x - q // 4) % 4
        return k2 * 4 + k1
    return slab, pos


def body(coefficients, alpha_pattern, alpha_count, alpha_blocks, beta_pattern, beta_count, beta_blocks):
    coeff_bf = coefficients.astype(jnp.bfloat16)
    slots = alpha_blocks.shape[1]
    alpha_mask = slot_mask(alpha_count, slots).astype(jnp.bfloat16)
    beta_mask = slot_mask(beta_count, slots).astype(jnp.bfloat16)
    rslab, rpos = row_tiles(coeff_bf)
    cslab, cpos = col_tiles(coeff_bf)
    a_picked = rslab[rpos(alpha_pattern[0])]
    b_picked = cslab[cpos(beta_pattern[0])]
    a_w = alpha_blocks[0] * alpha_mask[0][:, None, None]
    b_w = beta_blocks[0] * beta_mask[0][:, None, None]
    alpha_term = jnp.einsum("tab,tbn->an", a_w, a_picked, preferred_element_type=jnp.float32)
    beta_term = jnp.einsum("tak,tck->ac", b_picked, b_w, preferred_element_type=jnp.float32)
    return alpha_term + beta_term


def solution(mesh):
    fine = Mesh(mesh.devices.reshape(2, 4, 2, 4, 4), ROW + COL)
    placed = (P(ROW, COL), P(ROW, None), P(ROW), P(ROW, None, None, None), P(COL, None), P(COL), P(COL, None, None, None))
    return jax.shard_map(body, mesh=fine, in_specs=placed, out_specs=P(ROW, COL), check_vma=False)
```

```python
import jax
import jax.numpy as jnp
from jax import lax
from jax.sharding import Mesh, PartitionSpec as P

ROW = ("zh", "y", "core")
COL = ("x", "zl")


def shift(x, axis, s):
    n = lax.axis_size(axis)
    return lax.ppermute(x, axis, [(i, (i + s) % n) for i in range(n)])


def inverse_slots(pos_of_slot, count, npos):
    slots = pos_of_slot.shape[0]
    used = jnp.arange(slots, dtype=jnp.int32) < count
    match = (pos_of_slot[None, :] == jnp.arange(npos, dtype=jnp.int32)[:, None]) & used[None, :]
    valid = jnp.any(match, axis=1).astype(jnp.float32)
    slot = jnp.argmax(match, axis=1).astype(jnp.int32)
    return slot, valid


def body(coefficients, alpha_pattern, alpha_count, alpha_blocks, beta_pattern, beta_count, beta_blocks):
    t = coefficients.astype(jnp.bfloat16)
    zh = lax.axis_index("zh"); y = lax.axis_index("y"); core = lax.axis_index("core")
    x = lax.axis_index("x"); zl = lax.axis_index("zl")
    ny = lax.axis_size("y"); nx = lax.axis_size("x"); nzl = lax.axis_size("zl")

    pa = []
    u = shift(t, "zh", 1)
    pa += [(0, t), (1, u)]
    yt = [shift(t, "y", s) for s in range(1, ny)]
    yu = [shift(u, "y", s) for s in range(1, ny)]
    pa += [(s * 2, yt[s - 1]) for s in range(1, ny)]
    pa += [(s * 2 + 1, yu[s - 1]) for s in range(1, ny)]
    c0 = shift(jnp.stack([t, u]), "core", 1)
    c1 = shift(jnp.stack(yt), "core", 1)
    c2 = shift(jnp.stack(yu), "core", 1)
    pa += [(8, c0[0]), (9, c0[1])]
    pa += [(8 + s * 2, c1[s - 1]) for s in range(1, ny)]
    pa += [(8 + s * 2 + 1, c2[s - 1]) for s in range(1, ny)]
    p = alpha_pattern[0]
    apos = ((p % 2) ^ core) * 8 + ((y - (p // 2) % ny) % ny) * 2 + ((p // 8) ^ zh)
    aslot, avalid = inverse_slots(apos, alpha_count[0], 16)

    pb = [(0, t)]
    zt = [shift(t, "zl", s) for s in range(1, nzl)]
    pb += [(s, zt[s - 1]) for s in range(1, nzl)]
    zs = jnp.stack(zt)
    for s2 in range(1, nx):
        pb.append((s2 * 4, shift(t, "x", s2)))
        xz = shift(zs, "x", s2)
        pb += [(s2 * 4 + s, xz[s - 1]) for s in range(1, nzl)]
    q = beta_pattern[0]
    bpos = ((x - q // nzl) % nx) * 4 + ((zl - q % nzl) % nzl)
    bslot, bvalid = inverse_slots(bpos, beta_count[0], 16)

    ablk = alpha_blocks[0]
    bblk = beta_blocks[0]
    acc = jnp.zeros(t.shape, jnp.float32)
    for pos, tile in pa:
        w = lax.dynamic_index_in_dim(ablk, aslot[pos], 0, keepdims=False)
        acc = acc + avalid[pos] * jnp.dot(w, tile, preferred_element_type=jnp.float32)
    for pos, tile in pb:
        w = lax.dynamic_index_in_dim(bblk, bslot[pos], 0, keepdims=False)
        prod = lax.dot_general(tile, w, (((1,), (1,)), ((), ())), preferred_element_type=jnp.float32)
        acc = acc + bvalid[pos] * prod
    return acc


def solution(mesh):
    fine = Mesh(mesh.devices.reshape(2, 4, 2, 4, 4), ROW + COL)
    placed = (P(ROW, COL), P(ROW, None), P(ROW), P(ROW, None, None, None), P(COL, None), P(COL), P(COL, None, None, None))
    return jax.shard_map(body, mesh=fine, in_specs=placed, out_specs=P(ROW, COL), check_vma=False)
```

```python
import jax
import jax.numpy as jnp
from jax import lax
from jax.sharding import Mesh, PartitionSpec as P

ROW = ("zh", "y", "core")
COL = ("x", "zl")


def shift(x, axis, s):
    n = lax.axis_size(axis)
    return lax.ppermute(x, axis, [(i, (i + s) % n) for i in range(n)])


def inverse_slots(pos_of_slot, count, npos):
    slots = pos_of_slot.shape[0]
    used = jnp.arange(slots, dtype=jnp.int32) < count
    match = (pos_of_slot[None, :] == jnp.arange(npos, dtype=jnp.int32)[:, None]) & used[None, :]
    valid = jnp.any(match, axis=1)
    slot = jnp.argmax(match, axis=1).astype(jnp.int32)
    return slot, valid


def body(coefficients, alpha_pattern, alpha_count, alpha_blocks, beta_pattern, beta_count, beta_blocks):
    t = coefficients.astype(jnp.bfloat16)
    zh = lax.axis_index("zh"); y = lax.axis_index("y"); core = lax.axis_index("core")
    x = lax.axis_index("x"); zl = lax.axis_index("zl")
    ny = lax.axis_size("y"); nx = lax.axis_size("x"); nzl = lax.axis_size("zl")

    u = shift(t, "zh", 1)
    tu = jnp.stack([t, u])
    yt = jnp.stack([shift(t, "y", s) for s in range(1, ny)])
    yu = jnp.stack([shift(u, "y", s) for s in range(1, ny)])
    c0 = shift(tu, "core", 1)
    c1 = shift(yt, "core", 1)
    c2 = shift(yu, "core", 1)
    ga = [([0, 1], tu), ([2, 4, 6], yt), ([3, 5, 7], yu), ([8, 9], c0), ([10, 12, 14], c1), ([11, 13, 15], c2)]
    p = alpha_pattern[0]
    apos = ((p % 2) ^ core) * 8 + ((y - (p // 2) % ny) % ny) * 2 + ((p // 8) ^ zh)
    aslot, avalid = inverse_slots(apos, alpha_count[0], 16)
    wa = alpha_blocks[0][aslot] * avalid.astype(jnp.bfloat16)[:, None, None]

    zs = jnp.stack([shift(t, "zl", s) for s in range(1, nzl)])
    gb = [([0], t[None]), ([1, 2, 3], zs)]
    for s2 in range(1, nx):
        gb.append(([s2 * 4], shift(t, "x", s2)[None]))
        gb.append(([s2 * 4 + s for s in range(1, nzl)], shift(zs, "x", s2)))
    q = beta_pattern[0]
    bpos = ((x - q // nzl) % nx) * 4 + ((zl - q % nzl) % nzl)
    bslot, bvalid = inverse_slots(bpos, beta_count[0], 16)
    wb = beta_blocks[0][bslot] * bvalid.astype(jnp.bfloat16)[:, None, None]

    def pick(w, ps):
        if len(ps) == 1:
            return w[ps[0]:ps[0] + 1]
        step = ps[1] - ps[0]
        return w[ps[0]:ps[-1] + 1:step]

    acc = jnp.zeros(t.shape, jnp.float32)
    for ps, tiles in ga:
        acc = acc + jnp.einsum("tab,tbn->an", pick(wa, ps), tiles, preferred_element_type=jnp.float32)
    for ps, tiles in gb:
        acc = acc + jnp.einsum("tak,tck->ac", tiles, pick(wb, ps), preferred_element_type=jnp.float32)
    return acc


def solution(mesh):
    fine = Mesh(mesh.devices.reshape(2, 4, 2, 4, 4), ROW + COL)
    placed = (P(ROW, COL), P(ROW, None), P(ROW), P(ROW, None, None, None), P(COL, None), P(COL), P(COL, None, None, None))
    return jax.shard_map(body, mesh=fine, in_specs=placed, out_specs=P(ROW, COL), check_vma=False)
```

```python
import jax
import jax.numpy as jnp
from jax import lax
from jax.sharding import Mesh, PartitionSpec as P

ROW = ("zh", "y", "core")
COL = ("x", "zl")


def shift(x, axis, s):
    n = lax.axis_size(axis)
    return lax.ppermute(x, axis, [(i, (i + s) % n) for i in range(n)])


def inverse_slots(pos_of_slot, count, npos):
    slots = pos_of_slot.shape[0]
    used = jnp.arange(slots, dtype=jnp.int32) < count
    match = (pos_of_slot[None, :] == jnp.arange(npos, dtype=jnp.int32)[:, None]) & used[None, :]
    valid = jnp.any(match, axis=1)
    slot = jnp.argmax(match, axis=1).astype(jnp.int32)
    return slot, valid


def body(coefficients, alpha_pattern, alpha_count, alpha_blocks, beta_pattern, beta_count, beta_blocks):
    t = coefficients.astype(jnp.bfloat16)
    zh = lax.axis_index("zh"); y = lax.axis_index("y"); core = lax.axis_index("core")
    x = lax.axis_index("x"); zl = lax.axis_index("zl")
    ny = lax.axis_size("y"); nx = lax.axis_size("x"); nzl = lax.axis_size("zl")

    zs = jnp.stack([shift(t, "zl", s) for s in range(1, nzl)])
    t_late, zs = lax.optimization_barrier((t, zs))
    u = shift(t_late, "zh", 1)
    tu = jnp.stack([t, u])
    yt = jnp.stack([shift(t, "y", s) for s in range(1, ny)])
    yu = jnp.stack([shift(u, "y", s) for s in range(1, ny)])
    c0 = shift(tu, "core", 1)
    c1 = shift(yt, "core", 1)
    c2 = shift(yu, "core", 1)
    ga = [([0, 1], tu), ([2, 4, 6], yt), ([3, 5, 7], yu), ([8, 9], c0), ([10, 12, 14], c1), ([11, 13, 15], c2)]
    p = alpha_pattern[0]
    apos = ((p % 2) ^ core) * 8 + ((y - (p // 2) % ny) % ny) * 2 + ((p // 8) ^ zh)
    aslot, avalid = inverse_slots(apos, alpha_count[0], 16)
    wa = alpha_blocks[0][aslot] * avalid.astype(jnp.bfloat16)[:, None, None]

    gb = [([0], t[None]), ([1, 2, 3], zs)]
    for s2 in range(1, nx):
        gb.append(([s2 * 4], shift(t, "x", s2)[None]))
        gb.append(([s2 * 4 + s for s in range(1, nzl)], shift(zs, "x", s2)))
    q = beta_pattern[0]
    bpos = ((x - q // nzl) % nx) * 4 + ((zl - q % nzl) % nzl)
    bslot, bvalid = inverse_slots(bpos, beta_count[0], 16)
    wb = beta_blocks[0][bslot] * bvalid.astype(jnp.bfloat16)[:, None, None]

    def pick(w, ps):
        if len(ps) == 1:
            return w[ps[0]:ps[0] + 1]
        step = ps[1] - ps[0]
        return w[ps[0]:ps[-1] + 1:step]

    acc = jnp.zeros(t.shape, jnp.float32)
    for ps, tiles in ga:
        acc = acc + jnp.einsum("tab,tbn->an", pick(wa, ps), tiles, preferred_element_type=jnp.float32)
    for ps, tiles in gb:
        acc = acc + jnp.einsum("tak,tck->ac", tiles, pick(wb, ps), preferred_element_type=jnp.float32)
    return acc


def solution(mesh):
    fine = Mesh(mesh.devices.reshape(2, 4, 2, 4, 4), ROW + COL)
    placed = (P(ROW, COL), P(ROW, None), P(ROW), P(ROW, None, None, None), P(COL, None), P(COL), P(COL, None, None, None))
    return jax.shard_map(body, mesh=fine, in_specs=placed, out_specs=P(ROW, COL), check_vma=False)
```

```python
import jax
import jax.numpy as jnp
from jax import lax
from jax.sharding import Mesh, PartitionSpec as P

ROW = ("zh", "y", "core")
COL = ("x", "zl")


def shift(x, axis, s):
    n = lax.axis_size(axis)
    return lax.ppermute(x, axis, [(i, (i + s) % n) for i in range(n)])


def inverse_slots(pos_of_slot, count, npos):
    slots = pos_of_slot.shape[0]
    used = jnp.arange(slots, dtype=jnp.int32) < count
    match = (pos_of_slot[None, :] == jnp.arange(npos, dtype=jnp.int32)[:, None]) & used[None, :]
    valid = jnp.any(match, axis=1)
    slot = jnp.argmax(match, axis=1).astype(jnp.int32)
    return slot, valid


def body(coefficients, alpha_pattern, alpha_count, alpha_blocks, beta_pattern, beta_count, beta_blocks):
    t = coefficients.astype(jnp.bfloat16)
    zh = lax.axis_index("zh"); y = lax.axis_index("y"); core = lax.axis_index("core")
    x = lax.axis_index("x"); zl = lax.axis_index("zl")
    ny = lax.axis_size("y"); nx = lax.axis_size("x"); nzl = lax.axis_size("zl")

    half = t.shape[0] // 2
    zs1 = jnp.stack([shift(t[:half], "zl", s) for s in range(1, nzl)])
    t_bot, zs1 = lax.optimization_barrier((t[half:], zs1))
    zs2 = jnp.stack([shift(t_bot, "zl", s) for s in range(1, nzl)])
    t_late, zs2 = lax.optimization_barrier((t, zs2))
    u = shift(t_late, "zh", 1)
    tu = jnp.stack([t, u])
    yt = jnp.stack([shift(t, "y", s) for s in range(1, ny)])
    yu = jnp.stack([shift(u, "y", s) for s in range(1, ny)])
    c0 = shift(tu, "core", 1)
    c1 = shift(yt, "core", 1)
    c2 = shift(yu, "core", 1)
    ga = [([0, 1], tu), ([2, 4, 6], yt), ([3, 5, 7], yu), ([8, 9], c0), ([10, 12, 14], c1), ([11, 13, 15], c2)]
    p = alpha_pattern[0]
    apos = ((p % 2) ^ core) * 8 + ((y - (p // 2) % ny) % ny) * 2 + ((p // 8) ^ zh)
    aslot, avalid = inverse_slots(apos, alpha_count[0], 16)
    wa = alpha_blocks[0][aslot] * avalid.astype(jnp.bfloat16)[:, None, None]

    gb = [([0], t[None])]
    gh = [([1, 2, 3], zs1, zs2)]
    for s2 in range(1, nx):
        gb.append(([s2 * 4], shift(t, "x", s2)[None]))
        gh.append(([s2 * 4 + s for s in range(1, nzl)], shift(zs1, "x", s2), shift(zs2, "x", s2)))
    q = beta_pattern[0]
    bpos = ((x - q // nzl) % nx) * 4 + ((zl - q % nzl) % nzl)
    bslot, bvalid = inverse_slots(bpos, beta_count[0], 16)
    wb = beta_blocks[0][bslot] * bvalid.astype(jnp.bfloat16)[:, None, None]

    def pick(w, ps):
        if len(ps) == 1:
            return w[ps[0]:ps[0] + 1]
        step = ps[1] - ps[0]
        return w[ps[0]:ps[-1] + 1:step]

    acc = jnp.zeros(t.shape, jnp.float32)
    for ps, tiles in ga:
        acc = acc + jnp.einsum("tab,tbn->an", pick(wa, ps), tiles, preferred_element_type=jnp.float32)
    for ps, tiles in gb:
        acc = acc + jnp.einsum("tak,tck->ac", tiles, pick(wb, ps), preferred_element_type=jnp.float32)
    top = jnp.zeros((half, t.shape[1]), jnp.float32)
    bot = jnp.zeros((t.shape[0] - half, t.shape[1]), jnp.float32)
    for ps, tiles1, tiles2 in gh:
        w = pick(wb, ps)
        top = top + jnp.einsum("tak,tck->ac", tiles1, w, preferred_element_type=jnp.float32)
        bot = bot + jnp.einsum("tak,tck->ac", tiles2, w, preferred_element_type=jnp.float32)
    return acc + jnp.concatenate([top, bot], axis=0)


def solution(mesh):
    fine = Mesh(mesh.devices.reshape(2, 4, 2, 4, 4), ROW + COL)
    placed = (P(ROW, COL), P(ROW, None), P(ROW), P(ROW, None, None, None), P(COL, None), P(COL), P(COL, None, None, None))
    return jax.shard_map(body, mesh=fine, in_specs=placed, out_specs=P(ROW, COL), check_vma=False)
```

```python
import jax
import jax.numpy as jnp
from jax import lax
from jax.sharding import Mesh, PartitionSpec as P

ROW = ("zh", "y", "core")
COL = ("x", "zl")


def shift(x, axis, s):
    n = lax.axis_size(axis)
    return lax.ppermute(x, axis, [(i, (i + s) % n) for i in range(n)])


def inverse_slots(pos_of_slot, count, npos):
    slots = pos_of_slot.shape[0]
    used = jnp.arange(slots, dtype=jnp.int32) < count
    match = (pos_of_slot[None, :] == jnp.arange(npos, dtype=jnp.int32)[:, None]) & used[None, :]
    valid = jnp.any(match, axis=1)
    slot = jnp.argmax(match, axis=1).astype(jnp.int32)
    return slot, valid


def body(coefficients, alpha_pattern, alpha_count, alpha_blocks, beta_pattern, beta_count, beta_blocks):
    t = coefficients.astype(jnp.bfloat16)
    zh = lax.axis_index("zh"); y = lax.axis_index("y"); core = lax.axis_index("core")
    x = lax.axis_index("x"); zl = lax.axis_index("zl")
    ny = lax.axis_size("y"); nx = lax.axis_size("x"); nzl = lax.axis_size("zl")

    half = (t.shape[0] * 5) // 8
    zs1 = jnp.stack([shift(t[:half], "zl", s) for s in range(1, nzl)])
    t_bot, zs1 = lax.optimization_barrier((t[half:], zs1))
    zs2 = jnp.stack([shift(t_bot, "zl", s) for s in range(1, nzl)])
    t_late, zs2 = lax.optimization_barrier((t, zs2))
    u = shift(t_late, "zh", 1)
    tu = jnp.stack([t, u])
    yt = jnp.stack([shift(t, "y", s) for s in range(1, ny)])
    yu = jnp.stack([shift(u, "y", s) for s in range(1, ny)])
    c0 = shift(tu, "core", 1)
    c1 = shift(yt, "core", 1)
    c2 = shift(yu, "core", 1)
    ga = [([0, 1], tu), ([2, 4, 6], yt), ([3, 5, 7], yu), ([8, 9], c0), ([10, 12, 14], c1), ([11, 13, 15], c2)]
    p = alpha_pattern[0]
    apos = ((p % 2) ^ core) * 8 + ((y - (p // 2) % ny) % ny) * 2 + ((p // 8) ^ zh)
    aslot, avalid = inverse_slots(apos, alpha_count[0], 16)
    wa = alpha_blocks[0][aslot] * avalid.astype(jnp.bfloat16)[:, None, None]

    gb = [([0], t[None])]
    gh = [([1, 2, 3], zs1, zs2)]
    for s2 in range(1, nx):
        gb.append(([s2 * 4], shift(t, "x", s2)[None]))
        gh.append(([s2 * 4 + s for s in range(1, nzl)], shift(zs1, "x", s2), shift(zs2, "x", s2)))
    q = beta_pattern[0]
    bpos = ((x - q // nzl) % nx) * 4 + ((zl - q % nzl) % nzl)
    bslot, bvalid = inverse_slots(bpos, beta_count[0], 16)
    wb = beta_blocks[0][bslot] * bvalid.astype(jnp.bfloat16)[:, None, None]

    def pick(w, ps):
        if len(ps) == 1:
            return w[ps[0]:ps[0] + 1]
        step = ps[1] - ps[0]
        return w[ps[0]:ps[-1] + 1:step]

    acc = jnp.zeros(t.shape, jnp.float32)
    for ps, tiles in ga:
        acc = acc + jnp.einsum("tab,tbn->an", pick(wa, ps), tiles, preferred_element_type=jnp.float32)
    for ps, tiles in gb:
        acc = acc + jnp.einsum("tak,tck->ac", tiles, pick(wb, ps), preferred_element_type=jnp.float32)
    top = jnp.zeros((half, t.shape[1]), jnp.float32)
    bot = jnp.zeros((t.shape[0] - half, t.shape[1]), jnp.float32)
    for ps, tiles1, tiles2 in gh:
        w = pick(wb, ps)
        top = top + jnp.einsum("tak,tck->ac", tiles1, w, preferred_element_type=jnp.float32)
        bot = bot + jnp.einsum("tak,tck->ac", tiles2, w, preferred_element_type=jnp.float32)
    return acc + jnp.concatenate([top, bot], axis=0)


def solution(mesh):
    fine = Mesh(mesh.devices.reshape(2, 4, 2, 4, 4), ROW + COL)
    placed = (P(ROW, COL), P(ROW, None), P(ROW), P(ROW, None, None, None), P(COL, None), P(COL), P(COL, None, None, None))
    return jax.shard_map(body, mesh=fine, in_specs=placed, out_specs=P(ROW, COL), check_vma=False)
```
